512 devices in a mesh: sec: 2 (over core), section: 4 (over z_hi), expert: 64 (over y, x, z_lo).
Axes of the slice: x: 4, y: 4, z: 16 (z_hi: 4, z_lo: 4; z = z_hi * 4 + z_lo), core: 2. Of those that a mesh axis runs over, the one named last changes fastest.
Arguments:
- tokens: bfloat16 [8192, 2048], P('expert', ('sec', 'section')), may hold values from -6 to 6
- cotangent: bfloat16 [8192, 2048], P('expert', ('sec', 'section')), may hold values from -6 to 6
- expert_ids: int32 [8192, 2], P('expert'), may hold values from 0 to 63, all different within a row; in each aligned block of 128 rows (0 to 127, 128 to 255, ...) at most 6 rows name the same one
- gate_values: float32 [8192, 2], P('expert'), may hold values from 0.2 to 1
- expand_weight: bfloat16 [64, 2048, 4096], P('expert', None, ('sec', 'section')), may hold values from -0.125 to 0.125
- contract_weight: bfloat16 [64, 4096, 2048], P('expert', ('sec', 'section')), may hold values from -0.09375 to 0.09375
Outputs:
- combined: bfloat16 [8192, 2048], P('expert', ('sec', 'section'))
- input_grad: bfloat16 [8192, 2048], P('expert', ('sec', 'section'))
- gate_grad: float32 [8192, 2], P('expert')
The draws below stay inside these ranges and needn't reach their ends.
Inputs may be any that keep to these rules, and one draw needn't show every extreme that they name: `expert_ids`: the two ids of a token differ. Among the 128 tokens of one index of expert, no expert is named by more than 6 of them, a bound that some block reaches.
All inputs are finite; a program needn't handle non-finite values.
Results may differ from the reference program's by a relative error of at most 0.015.
Values may be sent and summed in bfloat16 or wider, within the bound.
No kernel may reach another device: no remote copies, remote signals or barrier semaphores. Data moves between devices by JAX's collectives and lax.ppermute only.
A program may use at most 64 MiB of HBM per device.

```python
import math
from functools import partial
import jax
import jax.numpy as jnp
import numpy as np
from jax import lax

D = 2048
FF = 4096
TOK_DEV = 128
EXPERTS = 64
TOKENS = 8192
CAP = 6
N_SEC = 2
N_SECTION = 4
N_EXPERT = 64


def levels(rng, extent, cuts, smallest, largest):
    def one(axis_at, blocks):
        steps = jax.random.uniform(jax.random.fold_in(jax.random.fold_in(rng, 6), axis_at), (blocks,), jnp.float32, smallest / len(cuts), largest / len(cuts))
        return jnp.repeat(jnp.exp(steps), extent[axis_at] // blocks).reshape((-1,) + (1,) * (len(extent) - axis_at - 1))

    gain = one(*cuts[0])
    for cut in cuts[1:]:
        gain = gain * one(*cut)
    return gain


def routed_block(rng, own, number, rows, number_of, top, bound, lean):
    order = jax.random.permutation(rng, number_of)
    crowded, usual = portions_of(number_of, rows * top, bound, lean, True), portions_of(number_of, rows * top, bound, lean, False)
    places = jnp.arange(number_of)

    def named(tallies, turn):
        used = int((tallies > 0).sum())
        fixed = max(1, used // 4)
        moved = fixed + (places - fixed + turn * (used - fixed)) % max(1, number_of - fixed)
        return jnp.zeros((number_of,), jnp.int32).at[order[jnp.where(places < fixed, places, moved)]].set(jnp.asarray(tallies, jnp.int32))

    tallies = jnp.where(number % 4 == 0, named(crowded, number // 4), named(usual, number - number // 4 - 1))
    mixed = jax.random.permutation(jax.random.fold_in(own, 3), number_of)
    source_of, receiver = mixed[0:number_of // 2 * 2:2], mixed[1:number_of // 2 * 2:2]
    room = jnp.minimum(tallies[source_of] - 1, bound - tallies[receiver]) // 2
    room = jnp.where((source_of == order[0]) | (receiver == order[0]) | (tallies[receiver] == 0), 0, jnp.maximum(room, 0))
    moved = jax.random.randint(jax.random.fold_in(own, 4), (number_of // 2,), 0, 1 << 20) % (room + 1)
    tallies = tallies.at[source_of].add(-moved).at[receiver].add(moved)
    members = jnp.searchsorted(jnp.cumsum(tallies), jnp.arange(rows * top), side="right").astype(jnp.int32)
    listing = members.reshape(top, rows).T
    listing = listing[jax.random.permutation(jax.random.fold_in(own, 1), rows)]
    turn = jax.random.randint(jax.random.fold_in(own, 2), (rows, 1), 0, top)
    return jnp.take_along_axis(listing, (jnp.arange(top)[None, :] + turn) % top, axis=1)


def portions_of(count, total, reach, lean, full):
    weights = [(1 << 20) // math.isqrt(standing ** lean) + 1 for standing in range(1, count + 1)]
    largest = reach if full else min(reach, max(-(-total // count), total * weights[0] // sum(weights)))
    least = 1 if total - largest >= count - 1 else 0
    counts, surplus = [largest] + [least] * (count - 1), total - largest - least * (count - 1)
    while surplus > 0:
        free = [i for i in range(1, count) if counts[i] < largest] or [i for i in range(1, count) if counts[i] < reach]
        mass, left = sum([weights[i] for i in free]), surplus
        for i in free:
            more = min(reach - counts[i], max(1, left * weights[i] // mass), surplus)
            counts[i] = counts[i] + more
            surplus = surplus - more
    return np.array(counts)


def scatter_about(rng, shape, width, most, cuts=(), kind=jnp.bfloat16):
    result = width * jax.random.normal(rng, shape, jnp.float32)
    if cuts:
        result = result * levels(rng, shape, cuts, -0.22, 0.18)
    return jnp.clip(result, -most, most).astype(kind)


def setup_inputs(seed: int = 0) -> dict:
    seeds = jax.random.split(jax.random.key(seed), 7)
    tokens = scatter_about(seeds[0], (TOKENS, D), 1.0, 6.0, ((0, 64), (1, 8)))
    cotangent = scatter_about(seeds[1], (TOKENS, D), 1.0, 6.0, ((0, 64), (1, 8)))
    expert_ids_keys = jax.random.split(jax.random.fold_in(seeds[2], 1), TOKENS // TOK_DEV)
    expert_ids_turns = jax.random.permutation(jax.random.fold_in(seeds[2], 3), TOKENS // TOK_DEV)
    expert_ids = jax.vmap(lambda own, number: routed_block(jax.random.fold_in(seeds[2], 2), own, number, TOK_DEV, EXPERTS, 2, CAP, 2))(expert_ids_keys, expert_ids_turns).reshape((TOKENS, 2))
    gate_values = jnp.clip(0.2 + 0.8 * jax.random.uniform(seeds[3], (TOKENS, 2), jnp.float32) ** levels(seeds[3], (TOKENS, 2), ((0, 64),), -0.2, 0.2), 0.2, 1.0)
    expand_weight = scatter_about(seeds[4], (EXPERTS, D, FF), D ** -0.5, 0.125, ((0, 64), (2, 8)))
    contract_weight = scatter_about(seeds[5], (EXPERTS, FF, D), FF ** -0.5, 0.09375, ((0, 64), (1, 8)))
    return {"tokens": tokens, "cotangent": cotangent, "expert_ids": expert_ids, "gate_values": gate_values, "expand_weight": expand_weight, "contract_weight": contract_weight}


gelu_coef = math.sqrt(2.0 / math.pi)
gelu_cubic = 0.044715

def gelu_parts(hidden):
    inner_arg = gelu_coef * (hidden + gelu_cubic * hidden * hidden * hidden)
    tanh_value = jnp.tanh(inner_arg)
    activation = 0.5 * hidden * (1.0 + tanh_value)
    derivative = 0.5 * (1.0 + tanh_value) + 0.5 * hidden * (1.0 - tanh_value * tanh_value) * gelu_coef * (1.0 + 3.0 * gelu_cubic * hidden * hidden)
    return (activation, derivative)

def slot_positions(expert_ids, capacity, experts):
    flat_ids = expert_ids.reshape(-1).astype(jnp.int32)
    one_hot = (flat_ids[:, None] == jnp.arange(experts, dtype=jnp.int32)[None, :]).astype(jnp.int32)
    earlier = lax.optimization_barrier(jnp.sum((jnp.cumsum(one_hot, axis=0) - one_hot) * one_hot, axis=1))
    return (flat_ids * capacity + earlier).astype(jnp.int32)

def reference(tokens, cotangent, expert_ids, gate_values, expand_weight, contract_weight):
    blocks = N_SEC * N_SECTION
    share = FF // blocks
    slot_count = N_EXPERT * CAP
    grouped = expert_ids.reshape(N_EXPERT, TOK_DEV, 2)
    positions = jax.vmap(partial(slot_positions, capacity=CAP, experts=EXPERTS))(grouped)
    source = jnp.arange(N_EXPERT, dtype=jnp.int32)[:, None]
    target_rows = (positions // CAP * slot_count + source * CAP + positions % CAP).astype(jnp.int32).reshape(-1)
    pairs_x = jnp.broadcast_to(tokens[:, None, :], (TOKENS, 2, D)).reshape(TOKENS * 2, D)
    scaled_grad = (gate_values[:, :, None] * cotangent[:, None, :].astype(jnp.float32)).astype(jnp.bfloat16)
    pairs_g = scaled_grad.reshape(TOKENS * 2, D)
    buffer_x = jnp.zeros((EXPERTS * slot_count, D), jnp.bfloat16).at[target_rows].set(pairs_x).reshape(EXPERTS, slot_count, D)
    buffer_g = jnp.zeros((EXPERTS * slot_count, D), jnp.bfloat16).at[target_rows].set(pairs_g).reshape(EXPERTS, slot_count, D)

    def expert_step(packed):
        rows_x, rows_g, w_expand, w_contract = packed
        hidden = jnp.dot(rows_x, w_expand, preferred_element_type=jnp.float32)
        activation, derivative = gelu_parts(hidden)
        activation = activation.astype(jnp.bfloat16)
        grad_activation = jnp.dot(rows_g, w_contract.T, preferred_element_type=jnp.float32)
        grad_hidden = (grad_activation * derivative).astype(jnp.bfloat16)
        act_blocks = activation.astype(jnp.float32).reshape(slot_count, blocks, share)
        contract_blocks = w_contract.astype(jnp.float32).reshape(blocks, share, D)
        out_terms = jnp.einsum('rbf,bfd->brd', act_blocks, contract_blocks).astype(jnp.bfloat16)
        out_terms = lax.optimization_barrier(out_terms).astype(jnp.float32)
        expert_out = lax.optimization_barrier(jnp.sum(out_terms, axis=0)).astype(jnp.bfloat16)
        grad_blocks = grad_hidden.astype(jnp.float32).reshape(slot_count, blocks, share)
        expand_blocks = w_expand.astype(jnp.float32).reshape(D, blocks, share)
        back_terms = jnp.einsum('rbf,dbf->brd', grad_blocks, expand_blocks).astype(jnp.bfloat16)
        back_terms = lax.optimization_barrier(back_terms).astype(jnp.float32)
        expert_back = lax.optimization_barrier(jnp.sum(back_terms, axis=0)).astype(jnp.bfloat16)
        return (expert_out, expert_back)
    outputs, backs = lax.map(expert_step, (buffer_x, buffer_g, expand_weight, contract_weight))
    out_pairs = outputs.reshape(EXPERTS * slot_count, D)[target_rows].astype(jnp.float32).reshape(TOKENS, 2, D)
    back_pairs = backs.reshape(EXPERTS * slot_count, D)[target_rows].astype(jnp.float32).reshape(TOKENS, 2, D)
    combined = lax.optimization_barrier(jnp.sum(gate_values[:, :, None] * out_pairs, axis=1)).astype(jnp.bfloat16)
    gate_grad = lax.optimization_barrier(jnp.sum(cotangent[:, None, :].astype(jnp.float32) * out_pairs, axis=2))
    input_grad = lax.optimization_barrier(jnp.sum(back_pairs, axis=1)).astype(jnp.bfloat16)
    return (combined, input_grad, gate_grad)
```

```python
import math

import jax
import jax.numpy as jnp
from jax import lax
from jax.sharding import PartitionSpec as P

gelu_coef = math.sqrt(2.0 / math.pi)
gelu_cubic = 0.044715


def gelu_parts(hidden):
    inner_arg = gelu_coef * (hidden + gelu_cubic * hidden * hidden * hidden)
    tanh_value = jnp.tanh(inner_arg)
    activation = 0.5 * hidden * (1.0 + tanh_value)
    derivative = 0.5 * (1.0 + tanh_value) + 0.5 * hidden * (
        1.0 - tanh_value * tanh_value
    ) * gelu_coef * (1.0 + 3.0 * gelu_cubic * hidden * hidden)
    return (activation, derivative)


def slot_positions(expert_ids, capacity, experts):
    flat_ids = expert_ids.reshape(-1)
    one_hot = (flat_ids[:, None] == jnp.arange(experts, dtype=jnp.int32)[None, :]).astype(jnp.int32)
    earlier = jnp.sum((jnp.cumsum(one_hot, axis=0) - one_hot) * one_hot, axis=1)
    return flat_ids * capacity + earlier


def transposed_product(left, right):
    return lax.dot_general(
        left, right, (((1,), (1,)), ((), ())), preferred_element_type=jnp.float32
    )


BLOCK_AXES = ("sec", "section")


def per_device(tokens, cotangent, expert_ids, gate_values, expand_weight, contract_weight):
    tok_rows, width_share = tokens.shape
    experts = lax.axis_size("expert")
    capacity = 3 * tok_rows // experts
    slot_count = experts * capacity
    expand_local = expand_weight[0]
    contract_local = contract_weight[0]
    full_width = contract_local.shape[1]
    positions = slot_positions(expert_ids, capacity, experts)
    placement_matrix = (
        positions[:, None] == jnp.arange(slot_count, dtype=jnp.int32)[None, :]
    ).astype(jnp.bfloat16)

    def to_slots(pairs):
        return jnp.dot(placement_matrix.T, pairs, preferred_element_type=jnp.float32).astype(
            jnp.bfloat16
        )

    whole_tokens = lax.all_gather(tokens, BLOCK_AXES, axis=1, tiled=True)
    whole_cot = lax.all_gather(cotangent, BLOCK_AXES, axis=1, tiled=True)
    whole_grad = (gate_values[:, :, None] * whole_cot[:, None, :].astype(jnp.float32)).astype(
        jnp.bfloat16
    )
    pair_tokens = jnp.broadcast_to(whole_tokens[:, None, :], (tok_rows, 2, full_width)).reshape(
        2 * tok_rows, full_width
    )
    send_x = to_slots(pair_tokens).reshape(experts, capacity, full_width)
    send_g = to_slots(whole_grad.reshape(2 * tok_rows, full_width)).reshape(
        experts, capacity, full_width
    )
    recv_x = lax.all_to_all(send_x, "expert", split_axis=0, concat_axis=0, tiled=True)
    hidden = jnp.dot(
        recv_x.reshape(slot_count, full_width), expand_local, preferred_element_type=jnp.float32
    )
    activation, derivative = gelu_parts(hidden)
    activation = activation.astype(jnp.bfloat16)
    out_part = jnp.dot(activation, contract_local, preferred_element_type=jnp.float32).astype(
        jnp.bfloat16
    )
    out_rows = lax.psum_scatter(out_part, BLOCK_AXES, scatter_dimension=1, tiled=True)
    returned_out = lax.all_to_all(
        out_rows.reshape(experts, capacity, width_share), "expert", split_axis=0, concat_axis=0,
        tiled=True,
    )

    recv_g = lax.all_to_all(send_g, "expert", split_axis=0, concat_axis=0, tiled=True)
    grad_activation = transposed_product(recv_g.reshape(slot_count, full_width), contract_local)
    grad_hidden = (grad_activation * derivative).astype(jnp.bfloat16)
    back_part = transposed_product(grad_hidden, expand_local).astype(jnp.bfloat16)
    back_rows = lax.psum_scatter(back_part, BLOCK_AXES, scatter_dimension=1, tiled=True)
    returned_back = lax.all_to_all(
        back_rows.reshape(experts, capacity, width_share), "expert", split_axis=0, concat_axis=0,
        tiled=True,
    )

    out_pairs = jnp.dot(
        placement_matrix,
        returned_out.reshape(slot_count, width_share),
        preferred_element_type=jnp.float32,
    ).reshape(tok_rows, 2, width_share)
    combined = jnp.sum(gate_values[:, :, None] * out_pairs, axis=1).astype(jnp.bfloat16)
    partial_dots = jnp.sum(cotangent[:, None, :].astype(jnp.float32) * out_pairs, axis=2)
    gate_grad = lax.psum(partial_dots, BLOCK_AXES)
    back_pairs = jnp.dot(
        placement_matrix,
        returned_back.reshape(slot_count, width_share),
        preferred_element_type=jnp.float32,
    ).reshape(tok_rows, 2, width_share)
    input_grad = (back_pairs[:, 0, :] + back_pairs[:, 1, :]).astype(jnp.bfloat16)
    return (combined, input_grad, gate_grad)


def solution(mesh):
    return jax.shard_map(
        per_device,
        mesh=mesh,
        in_specs=(
            P("expert", BLOCK_AXES),
            P("expert", BLOCK_AXES),
            P("expert", None),
            P("expert", None),
            P("expert", None, BLOCK_AXES),
            P("expert", BLOCK_AXES, None),
        ),
        out_specs=(
            P("expert", BLOCK_AXES),
            P("expert", BLOCK_AXES),
            P("expert", None),
        ),
        check_vma=False,
    )
```

```python
import math

import jax
import jax.numpy as jnp
from jax import lax
from jax.sharding import PartitionSpec as P

gelu_coef = math.sqrt(2.0 / math.pi)
gelu_cubic = 0.044715


def gelu_parts(hidden):
    inner_arg = gelu_coef * (hidden + gelu_cubic * hidden * hidden * hidden)
    tanh_value = jnp.tanh(inner_arg)
    activation = 0.5 * hidden * (1.0 + tanh_value)
    derivative = 0.5 * (1.0 + tanh_value) + 0.5 * hidden * (
        1.0 - tanh_value * tanh_value
    ) * gelu_coef * (1.0 + 3.0 * gelu_cubic * hidden * hidden)
    return (activation, derivative)


def slot_positions(expert_ids, capacity, experts):
    flat_ids = expert_ids.reshape(-1)
    one_hot = (flat_ids[:, None] == jnp.arange(experts, dtype=jnp.int32)[None, :]).astype(jnp.int32)
    earlier = jnp.sum((jnp.cumsum(one_hot, axis=0) - one_hot) * one_hot, axis=1)
    return flat_ids * capacity + earlier


def transposed_product(left, right):
    return lax.dot_general(
        left, right, (((1,), (1,)), ((), ())), preferred_element_type=jnp.float32
    )


BLOCK_AXES = ("sec", "section")


def per_device(tokens, cotangent, expert_ids, gate_values, expand_weight, contract_weight):
    tok_rows, width_share = tokens.shape
    experts = lax.axis_size("expert")
    capacity = 3 * tok_rows // experts
    slot_count = experts * capacity
    expand_local = expand_weight[0]
    contract_local = contract_weight[0]
    full_width = contract_local.shape[1]
    positions = slot_positions(expert_ids, capacity, experts)
    placement_matrix = (
        positions[:, None] == jnp.arange(slot_count, dtype=jnp.int32)[None, :]
    ).astype(jnp.bfloat16)

    def to_slots(pairs):
        return jnp.dot(placement_matrix.T, pairs, preferred_element_type=jnp.float32).astype(
            jnp.bfloat16
        )

    stacked = jnp.stack([tokens, cotangent], axis=1)
    whole_stacked = lax.all_gather(stacked, BLOCK_AXES, axis=2, tiled=True)
    whole_tokens = whole_stacked[:, 0, :]
    whole_cot = whole_stacked[:, 1, :]
    whole_grad = (gate_values[:, :, None] * whole_cot[:, None, :].astype(jnp.float32)).astype(
        jnp.bfloat16
    )
    pair_tokens = jnp.broadcast_to(whole_tokens[:, None, :], (tok_rows, 2, full_width)).reshape(
        2 * tok_rows, full_width
    )
    send_x = to_slots(pair_tokens).reshape(experts, capacity, full_width)
    send_g = to_slots(whole_grad.reshape(2 * tok_rows, full_width)).reshape(
        experts, capacity, full_width
    )
    recv_x = lax.all_to_all(send_x, "expert", split_axis=0, concat_axis=0, tiled=True)
    hidden = jnp.dot(
        recv_x.reshape(slot_count, full_width), expand_local, preferred_element_type=jnp.float32
    )
    activation, derivative = gelu_parts(hidden)
    activation = activation.astype(jnp.bfloat16)
    out_part = jnp.dot(activation, contract_local, preferred_element_type=jnp.float32).astype(
        jnp.bfloat16
    )
    send_g, out_part = lax.optimization_barrier((send_g, out_part))
    out_rows = lax.psum_scatter(out_part, BLOCK_AXES, scatter_dimension=1, tiled=True)
    recv_g = lax.all_to_all(send_g, "expert", split_axis=0, concat_axis=0, tiled=True)
    returned_out = lax.all_to_all(
        out_rows.reshape(experts, capacity, width_share), "expert", split_axis=0, concat_axis=0,
        tiled=True,
    )
    grad_activation = transposed_product(recv_g.reshape(slot_count, full_width), contract_local)
    grad_hidden = (grad_activation * derivative).astype(jnp.bfloat16)
    back_part = transposed_product(grad_hidden, expand_local).astype(jnp.bfloat16)
    back_rows = lax.psum_scatter(back_part, BLOCK_AXES, scatter_dimension=1, tiled=True)
    returned_back = lax.all_to_all(
        back_rows.reshape(experts, capacity, width_share), "expert", split_axis=0, concat_axis=0,
        tiled=True,
    )

    out_pairs = jnp.dot(
        placement_matrix,
        returned_out.reshape(slot_count, width_share),
        preferred_element_type=jnp.float32,
    ).reshape(tok_rows, 2, width_share)
    combined = jnp.sum(gate_values[:, :, None] * out_pairs, axis=1).astype(jnp.bfloat16)
    partial_dots = jnp.sum(cotangent[:, None, :].astype(jnp.float32) * out_pairs, axis=2)
    gate_grad = lax.psum(partial_dots, BLOCK_AXES)
    back_pairs = jnp.dot(
        placement_matrix,
        returned_back.reshape(slot_count, width_share),
        preferred_element_type=jnp.float32,
    ).reshape(tok_rows, 2, width_share)
    input_grad = (back_pairs[:, 0, :] + back_pairs[:, 1, :]).astype(jnp.bfloat16)
    return (combined, input_grad, gate_grad)


def solution(mesh):
    return jax.shard_map(
        per_device,
        mesh=mesh,
        in_specs=(
            P("expert", BLOCK_AXES),
            P("expert", BLOCK_AXES),
            P("expert", None),
            P("expert", None),
            P("expert", None, BLOCK_AXES),
            P("expert", BLOCK_AXES, None),
        ),
        out_specs=(
            P("expert", BLOCK_AXES),
            P("expert", BLOCK_AXES),
            P("expert", None),
        ),
        check_vma=False,
    )
```

```python
import math

import jax
import jax.numpy as jnp
from jax import lax
from jax.sharding import PartitionSpec as P

gelu_coef = math.sqrt(2.0 / math.pi)
gelu_cubic = 0.044715


def gelu_parts(hidden):
    inner_arg = gelu_coef * (hidden + gelu_cubic * hidden * hidden * hidden)
    tanh_value = jnp.tanh(inner_arg)
    activation = 0.5 * hidden * (1.0 + tanh_value)
    derivative = 0.5 * (1.0 + tanh_value) + 0.5 * hidden * (
        1.0 - tanh_value * tanh_value
    ) * gelu_coef * (1.0 + 3.0 * gelu_cubic * hidden * hidden)
    return (activation, derivative)


def slot_positions(expert_ids, capacity, experts):
    flat_ids = expert_ids.reshape(-1)
    one_hot = (flat_ids[:, None] == jnp.arange(experts, dtype=jnp.int32)[None, :]).astype(jnp.int32)
    earlier = jnp.sum((jnp.cumsum(one_hot, axis=0) - one_hot) * one_hot, axis=1)
    return flat_ids * capacity + earlier


def transposed_product(left, right):
    return lax.dot_general(
        left, right, (((1,), (1,)), ((), ())), preferred_element_type=jnp.float32
    )


BLOCK_AXES = ("sec", "section")


def per_device(tokens, cotangent, expert_ids, gate_values, expand_weight, contract_weight):
    tok_rows, width_share = tokens.shape
    experts = lax.axis_size("expert")
    capacity = 3 * tok_rows // experts
    slot_count = experts * capacity
    expand_local = expand_weight[0]
    contract_local = contract_weight[0]
    full_width = contract_local.shape[1]
    positions = slot_positions(expert_ids, capacity, experts)
    placement_matrix = (
        positions[:, None] == jnp.arange(slot_count, dtype=jnp.int32)[None, :]
    ).astype(jnp.bfloat16)

    def to_slots(pairs):
        return jnp.dot(placement_matrix.T, pairs, preferred_element_type=jnp.float32).astype(
            jnp.bfloat16
        )

    stacked = jnp.stack([tokens, cotangent], axis=1)
    whole_stacked = lax.all_gather(stacked, BLOCK_AXES, axis=2, tiled=True)
    whole_tokens = whole_stacked[:, 0, :]
    whole_cot = whole_stacked[:, 1, :]
    whole_grad = (gate_values[:, :, None] * whole_cot[:, None, :].astype(jnp.float32)).astype(
        jnp.bfloat16
    )
    pair_tokens = jnp.broadcast_to(whole_tokens[:, None, :], (tok_rows, 2, full_width)).reshape(
        2 * tok_rows, full_width
    )
    send_x = to_slots(pair_tokens).reshape(experts, capacity, full_width)
    send_g = to_slots(whole_grad.reshape(2 * tok_rows, full_width)).reshape(
        experts, capacity, full_width
    )
    recv_xg = lax.all_to_all(
        jnp.stack([send_x, send_g]), "expert", split_axis=1, concat_axis=1, tiled=True
    )
    recv_x = recv_xg[0]
    recv_g = recv_xg[1]
    hidden = jnp.dot(
        recv_x.reshape(slot_count, full_width), expand_local, preferred_element_type=jnp.float32
    )
    activation, derivative = gelu_parts(hidden)
    activation = activation.astype(jnp.bfloat16)
    out_part = jnp.dot(activation, contract_local, preferred_element_type=jnp.float32).astype(
        jnp.bfloat16
    )
    out_rows = lax.psum_scatter(out_part, BLOCK_AXES, scatter_dimension=1, tiled=True)
    returned_out = lax.all_to_all(
        out_rows.reshape(experts, capacity, width_share), "expert", split_axis=0, concat_axis=0,
        tiled=True,
    )
    grad_activation = transposed_product(recv_g.reshape(slot_count, full_width), contract_local)
    grad_hidden = (grad_activation * derivative).astype(jnp.bfloat16)
    back_part = transposed_product(grad_hidden, expand_local).astype(jnp.bfloat16)
    back_rows = lax.psum_scatter(back_part, BLOCK_AXES, scatter_dimension=1, tiled=True)
    out_pairs = jnp.dot(
        placement_matrix,
        returned_out.reshape(slot_count, width_share),
        preferred_element_type=jnp.float32,
    ).reshape(tok_rows, 2, width_share)
    combined = jnp.sum(gate_values[:, :, None] * out_pairs, axis=1).astype(jnp.bfloat16)
    partial_dots = jnp.sum(cotangent[:, None, :].astype(jnp.float32) * out_pairs, axis=2)
    gate_grad = lax.psum(partial_dots, BLOCK_AXES)
    gate_grad, back_rows = lax.optimization_barrier((gate_grad, back_rows))
    returned_back = lax.all_to_all(
        back_rows.reshape(experts, capacity, width_share), "expert", split_axis=0, concat_axis=0,
        tiled=True,
    )
    back_pairs = jnp.dot(
        placement_matrix,
        returned_back.reshape(slot_count, width_share),
        preferred_element_type=jnp.float32,
    ).reshape(tok_rows, 2, width_share)
    input_grad = (back_pairs[:, 0, :] + back_pairs[:, 1, :]).astype(jnp.bfloat16)
    return (combined, input_grad, gate_grad)


def solution(mesh):
    return jax.shard_map(
        per_device,
        mesh=mesh,
        in_specs=(
            P("expert", BLOCK_AXES),
            P("expert", BLOCK_AXES),
            P("expert", None),
            P("expert", None),
            P("expert", None, BLOCK_AXES),
            P("expert", BLOCK_AXES, None),
        ),
        out_specs=(
            P("expert", BLOCK_AXES),
            P("expert", BLOCK_AXES),
            P("expert", None),
        ),
        check_vma=False,
    )
```

```python
import math

import jax
import jax.numpy as jnp
from jax import lax
from jax.sharding import PartitionSpec as P

gelu_coef = math.sqrt(2.0 / math.pi)
gelu_cubic = 0.044715


def gelu_parts(hidden):
    inner_arg = gelu_coef * (hidden + gelu_cubic * hidden * hidden * hidden)
    tanh_value = jnp.tanh(inner_arg)
    activation = 0.5 * hidden * (1.0 + tanh_value)
    derivative = 0.5 * (1.0 + tanh_value) + 0.5 * hidden * (
        1.0 - tanh_value * tanh_value
    ) * gelu_coef * (1.0 + 3.0 * gelu_cubic * hidden * hidden)
    return (activation, derivative)


def slot_positions(expert_ids, capacity, experts):
    flat_ids = expert_ids.reshape(-1)
    one_hot = (flat_ids[:, None] == jnp.arange(experts, dtype=jnp.int32)[None, :]).astype(jnp.int32)
    earlier = jnp.sum((jnp.cumsum(one_hot, axis=0) - one_hot) * one_hot, axis=1)
    return flat_ids * capacity + earlier


def transposed_product(left, right):
    return lax.dot_general(
        left, right, (((1,), (1,)), ((), ())), preferred_element_type=jnp.float32
    )


BLOCK_AXES = ("sec", "section")


def per_device(tokens, cotangent, expert_ids, gate_values, expand_weight, contract_weight):
    tok_rows, width_share = tokens.shape
    experts = lax.axis_size("expert")
    capacity = 3 * tok_rows // experts
    slot_count = experts * capacity
    expand_local = expand_weight[0]
    contract_local = contract_weight[0]
    full_width = contract_local.shape[1]
    positions = slot_positions(expert_ids, capacity, experts)
    placement_matrix = (
        positions[:, None] == jnp.arange(slot_count, dtype=jnp.int32)[None, :]
    ).astype(jnp.bfloat16)

    def to_slots(pairs):
        return jnp.dot(placement_matrix.T, pairs, preferred_element_type=jnp.float32).astype(
            jnp.bfloat16
        )

    stacked = jnp.stack([tokens, cotangent], axis=1)
    whole_stacked = lax.all_gather(stacked, BLOCK_AXES, axis=2, tiled=True)
    whole_tokens = whole_stacked[:, 0, :]
    whole_cot = whole_stacked[:, 1, :]
    whole_grad = (gate_values[:, :, None] * whole_cot[:, None, :].astype(jnp.float32)).astype(
        jnp.bfloat16
    )
    pair_tokens = jnp.broadcast_to(whole_tokens[:, None, :], (tok_rows, 2, full_width)).reshape(
        2 * tok_rows, full_width
    )
    send_x = to_slots(pair_tokens).reshape(experts, capacity, full_width)
    send_g = to_slots(whole_grad.reshape(2 * tok_rows, full_width)).reshape(
        experts, capacity, full_width
    )
    lane = 128
    chunk_rows = capacity * full_width // lane
    send_xg = jnp.concatenate(
        [send_x.reshape(experts, chunk_rows, lane), send_g.reshape(experts, chunk_rows, lane)],
        axis=1,
    )
    recv_xg = lax.all_to_all(send_xg, "expert", split_axis=0, concat_axis=0, tiled=True)
    recv_x = recv_xg[:, :chunk_rows].reshape(slot_count, full_width)
    recv_g = recv_xg[:, chunk_rows:].reshape(slot_count, full_width)
    hidden = jnp.dot(
        recv_x.reshape(slot_count, full_width), expand_local, preferred_element_type=jnp.float32
    )
    activation, derivative = gelu_parts(hidden)
    activation = activation.astype(jnp.bfloat16)
    out_part = jnp.dot(activation, contract_local, preferred_element_type=jnp.float32).astype(
        jnp.bfloat16
    )
    out_rows = lax.psum_scatter(out_part, BLOCK_AXES, scatter_dimension=1, tiled=True)
    returned_out = lax.all_to_all(
        out_rows.reshape(experts, capacity, width_share), "expert", split_axis=0, concat_axis=0,
        tiled=True,
    )
    grad_activation = transposed_product(recv_g.reshape(slot_count, full_width), contract_local)
    grad_hidden = (grad_activation * derivative).astype(jnp.bfloat16)
    back_part = transposed_product(grad_hidden, expand_local).astype(jnp.bfloat16)
    back_rows = lax.psum_scatter(back_part, BLOCK_AXES, scatter_dimension=1, tiled=True)
    out_pairs = jnp.dot(
        placement_matrix,
        returned_out.reshape(slot_count, width_share),
        preferred_element_type=jnp.float32,
    ).reshape(tok_rows, 2, width_share)
    combined = jnp.sum(gate_values[:, :, None] * out_pairs, axis=1).astype(jnp.bfloat16)
    partial_dots = jnp.sum(cotangent[:, None, :].astype(jnp.float32) * out_pairs, axis=2)
    gate_grad = lax.psum(partial_dots, BLOCK_AXES)
    gate_grad, back_rows = lax.optimization_barrier((gate_grad, back_rows))
    returned_back = lax.all_to_all(
        back_rows.reshape(experts, capacity, width_share), "expert", split_axis=0, concat_axis=0,
        tiled=True,
    )
    back_pairs = jnp.dot(
        placement_matrix,
        returned_back.reshape(slot_count, width_share),
        preferred_element_type=jnp.float32,
    ).reshape(tok_rows, 2, width_share)
    input_grad = (back_pairs[:, 0, :] + back_pairs[:, 1, :]).astype(jnp.bfloat16)
    return (combined, input_grad, gate_grad)


def solution(mesh):
    return jax.shard_map(
        per_device,
        mesh=mesh,
        in_specs=(
            P("expert", BLOCK_AXES),
            P("expert", BLOCK_AXES),
            P("expert", None),
            P("expert", None),
            P("expert", None, BLOCK_AXES),
            P("expert", BLOCK_AXES, None),
        ),
        out_specs=(
            P("expert", BLOCK_AXES),
            P("expert", BLOCK_AXES),
            P("expert", None),
        ),
        check_vma=False,
    )
```

```python
import math

import jax
import jax.numpy as jnp
from jax import lax
from jax.sharding import PartitionSpec as P

gelu_coef = math.sqrt(2.0 / math.pi)
gelu_cubic = 0.044715


def gelu_parts(hidden):
    inner_arg = gelu_coef * (hidden + gelu_cubic * hidden * hidden * hidden)
    tanh_value = jnp.tanh(inner_arg)
    activation = 0.5 * hidden * (1.0 + tanh_value)
    derivative = 0.5 * (1.0 + tanh_value) + 0.5 * hidden * (
        1.0 - tanh_value * tanh_value
    ) * gelu_coef * (1.0 + 3.0 * gelu_cubic * hidden * hidden)
    return (activation, derivative)


def slot_positions(expert_ids, capacity, experts):
    flat_ids = expert_ids.reshape(-1)
    one_hot = (flat_ids[:, None] == jnp.arange(experts, dtype=jnp.int32)[None, :]).astype(jnp.int32)
    earlier = jnp.sum((jnp.cumsum(one_hot, axis=0) - one_hot) * one_hot, axis=1)
    return flat_ids * capacity + earlier


def transposed_product(left, right):
    return lax.dot_general(
        left, right, (((1,), (1,)), ((), ())), preferred_element_type=jnp.float32
    )


BLOCK_AXES = ("sec", "section")


def per_device(tokens, cotangent, expert_ids, gate_values, expand_weight, contract_weight):
    tok_rows, width_share = tokens.shape
    experts = lax.axis_size("expert")
    capacity = 3 * tok_rows // experts
    slot_count = experts * capacity
    expand_local = expand_weight[0]
    contract_local = contract_weight[0]
    full_width = contract_local.shape[1]
    positions = slot_positions(expert_ids, capacity, experts)
    placement_matrix = (
        positions[:, None] == jnp.arange(slot_count, dtype=jnp.int32)[None, :]
    ).astype(jnp.bfloat16)

    def to_slots(pairs):
        return jnp.dot(placement_matrix.T, pairs, preferred_element_type=jnp.float32).astype(
            jnp.bfloat16
        )

    stacked = jnp.stack([tokens, cotangent], axis=1)
    whole_stacked = lax.all_gather(stacked, BLOCK_AXES, axis=2, tiled=True)
    whole_tokens = whole_stacked[:, 0, :]
    whole_cot = whole_stacked[:, 1, :]
    whole_grad = (gate_values[:, :, None] * whole_cot[:, None, :].astype(jnp.float32)).astype(
        jnp.bfloat16
    )
    pair_tokens = jnp.broadcast_to(whole_tokens[:, None, :], (tok_rows, 2, full_width)).reshape(
        2 * tok_rows, full_width
    )
    send_x = to_slots(pair_tokens).reshape(experts, capacity, full_width)
    send_g = to_slots(whole_grad.reshape(2 * tok_rows, full_width)).reshape(
        experts, capacity, full_width
    )
    lane = 128
    chunk_rows = capacity * full_width // lane
    send_xg = jnp.concatenate(
        [send_x.reshape(experts, chunk_rows, lane), send_g.reshape(experts, chunk_rows, lane)],
        axis=1,
    )
    recv_xg = lax.all_to_all(send_xg, "expert", split_axis=0, concat_axis=0, tiled=True)
    recv_x = recv_xg[:, :chunk_rows].reshape(slot_count, full_width)
    recv_g = recv_xg[:, chunk_rows:].reshape(slot_count, full_width)
    hidden = jnp.dot(
        recv_x.reshape(slot_count, full_width), expand_local, preferred_element_type=jnp.float32
    )
    activation, derivative = gelu_parts(hidden)
    activation = activation.astype(jnp.bfloat16)
    out_part = jnp.dot(activation, contract_local, preferred_element_type=jnp.float32).astype(
        jnp.bfloat16
    )
    grad_activation = transposed_product(recv_g.reshape(slot_count, full_width), contract_local)
    grad_hidden = (grad_activation * derivative).astype(jnp.bfloat16)
    back_part = transposed_product(grad_hidden, expand_local).astype(jnp.bfloat16)
    out_part, back_part = lax.optimization_barrier((out_part, back_part))
    out_rows = lax.psum_scatter(out_part, BLOCK_AXES, scatter_dimension=1, tiled=True)
    block_count = full_width // width_share
    back_blocks = lax.all_to_all(
        back_part.reshape(slot_count, block_count, width_share), BLOCK_AXES, 1, 1, tiled=True
    )
    out_rows, back_blocks = lax.optimization_barrier((out_rows, back_blocks))
    back_rows = jnp.sum(back_blocks.astype(jnp.float32), axis=1).astype(jnp.bfloat16)
    returned_out = lax.all_to_all(
        out_rows.reshape(experts, capacity, width_share), "expert", split_axis=0, concat_axis=0,
        tiled=True,
    )
    out_pairs = jnp.dot(
        placement_matrix,
        returned_out.reshape(slot_count, width_share),
        preferred_element_type=jnp.float32,
    ).reshape(tok_rows, 2, width_share)
    combined = jnp.sum(gate_values[:, :, None] * out_pairs, axis=1).astype(jnp.bfloat16)
    partial_dots = jnp.sum(cotangent[:, None, :].astype(jnp.float32) * out_pairs, axis=2)
    gate_grad = lax.psum(partial_dots, BLOCK_AXES)
    returned_back = lax.all_to_all(
        back_rows.reshape(experts, capacity, width_share), "expert", split_axis=0, concat_axis=0,
        tiled=True,
    )
    back_pairs = jnp.dot(
        placement_matrix,
        returned_back.reshape(slot_count, width_share),
        preferred_element_type=jnp.float32,
    ).reshape(tok_rows, 2, width_share)
    input_grad = (back_pairs[:, 0, :] + back_pairs[:, 1, :]).astype(jnp.bfloat16)
    return (combined, input_grad, gate_grad)


def solution(mesh):
    return jax.shard_map(
        per_device,
        mesh=mesh,
        in_specs=(
            P("expert", BLOCK_AXES),
            P("expert", BLOCK_AXES),
            P("expert", None),
            P("expert", None),
            P("expert", None, BLOCK_AXES),
            P("expert", BLOCK_AXES, None),
        ),
        out_specs=(
            P("expert", BLOCK_AXES),
            P("expert", BLOCK_AXES),
            P("expert", None),
        ),
        check_vma=False,
    )
```

```python
import math

import jax
import jax.numpy as jnp
from jax import lax
from jax.sharding import PartitionSpec as P

gelu_coef = math.sqrt(2.0 / math.pi)
gelu_cubic = 0.044715


def gelu_parts(hidden):
    inner_arg = gelu_coef * (hidden + gelu_cubic * hidden * hidden * hidden)
    tanh_value = jnp.tanh(inner_arg)
    activation = 0.5 * hidden * (1.0 + tanh_value)
    derivative = 0.5 * (1.0 + tanh_value) + 0.5 * hidden * (
        1.0 - tanh_value * tanh_value
    ) * gelu_coef * (1.0 + 3.0 * gelu_cubic * hidden * hidden)
    return (activation, derivative)


def slot_positions(expert_ids, capacity, experts):
    flat_ids = expert_ids.reshape(-1)
    one_hot = (flat_ids[:, None] == jnp.arange(experts, dtype=jnp.int32)[None, :]).astype(jnp.int32)
    earlier = jnp.sum((jnp.cumsum(one_hot, axis=0) - one_hot) * one_hot, axis=1)
    return flat_ids * capacity + earlier


def transposed_product(left, right):
    return lax.dot_general(
        left, right, (((1,), (1,)), ((), ())), preferred_element_type=jnp.float32
    )


BLOCK_AXES = ("sec", "section")


def per_device(tokens, cotangent, expert_ids, gate_values, expand_weight, contract_weight):
    tok_rows, width_share = tokens.shape
    experts = lax.axis_size("expert")
    capacity = 3 * tok_rows // experts
    slot_count = experts * capacity
    expand_local = expand_weight[0]
    contract_local = contract_weight[0]
    full_width = contract_local.shape[1]
    positions = slot_positions(expert_ids, capacity, experts)
    placement_matrix = (
        positions[:, None] == jnp.arange(slot_count, dtype=jnp.int32)[None, :]
    ).astype(jnp.bfloat16)

    def to_slots(pairs):
        return jnp.dot(placement_matrix.T, pairs, preferred_element_type=jnp.float32).astype(
            jnp.bfloat16
        )

    stacked = jnp.stack([tokens, cotangent], axis=1)
    whole_stacked = lax.all_gather(stacked, BLOCK_AXES, axis=2, tiled=True)
    whole_tokens = whole_stacked[:, 0, :]
    whole_cot = whole_stacked[:, 1, :]
    whole_grad = (gate_values[:, :, None] * whole_cot[:, None, :].astype(jnp.float32)).astype(
        jnp.bfloat16
    )
    pair_tokens = jnp.broadcast_to(whole_tokens[:, None, :], (tok_rows, 2, full_width)).reshape(
        2 * tok_rows, full_width
    )
    send_x = to_slots(pair_tokens).reshape(experts, capacity, full_width)
    send_g = to_slots(whole_grad.reshape(2 * tok_rows, full_width)).reshape(
        experts, capacity, full_width
    )
    lane = 128
    chunk_rows = capacity * full_width // lane
    send_xg = jnp.concatenate(
        [send_x.reshape(experts, chunk_rows, lane), send_g.reshape(experts, chunk_rows, lane)],
        axis=1,
    )
    recv_xg = lax.all_to_all(send_xg, "expert", split_axis=0, concat_axis=0, tiled=True)
    recv_x = recv_xg[:, :chunk_rows].reshape(slot_count, full_width)
    recv_g = recv_xg[:, chunk_rows:].reshape(slot_count, full_width)
    hidden = jnp.dot(
        recv_x.reshape(slot_count, full_width), expand_local, preferred_element_type=jnp.float32
    )
    activation, derivative = gelu_parts(hidden)
    activation = activation.astype(jnp.bfloat16)
    out_part = jnp.dot(activation, contract_local, preferred_element_type=jnp.float32).astype(
        jnp.bfloat16
    )
    grad_activation = transposed_product(recv_g, contract_local)
    grad_hidden = (grad_activation * derivative).astype(jnp.bfloat16)
    back_part = transposed_product(grad_hidden, expand_local).astype(jnp.bfloat16)
    send_parts = jnp.concatenate(
        [out_part.reshape(experts, chunk_rows, lane), back_part.reshape(experts, chunk_rows, lane)],
        axis=1,
    )
    recv_parts = lax.all_to_all(send_parts, "expert", split_axis=0, concat_axis=0, tiled=True)
    returned_out = recv_parts[:, :chunk_rows].reshape(slot_count, full_width)
    returned_back = recv_parts[:, chunk_rows:].reshape(slot_count, full_width)
    out_pairs = jnp.dot(
        placement_matrix, returned_out, preferred_element_type=jnp.float32
    ).reshape(tok_rows, 2, full_width)
    back_pairs = jnp.dot(
        placement_matrix, returned_back, preferred_element_type=jnp.float32
    ).reshape(tok_rows, 2, full_width)
    combined_part = jnp.sum(gate_values[:, :, None] * out_pairs, axis=1)
    input_part = back_pairs[:, 0, :] + back_pairs[:, 1, :]
    partial_dots = jnp.sum(whole_cot[:, None, :].astype(jnp.float32) * out_pairs, axis=2)
    reduced = lax.psum_scatter(
        jnp.stack([combined_part, input_part]).astype(jnp.bfloat16),
        BLOCK_AXES,
        scatter_dimension=2,
        tiled=True,
    )
    gate_grad = lax.psum(partial_dots, BLOCK_AXES)
    combined = reduced[0]
    input_grad = reduced[1]
    return (combined, input_grad, gate_grad)


def solution(mesh):
    return jax.shard_map(
        per_device,
        mesh=mesh,
        in_specs=(
            P("expert", BLOCK_AXES),
            P("expert", BLOCK_AXES),
            P("expert", None),
            P("expert", None),
            P("expert", None, BLOCK_AXES),
            P("expert", BLOCK_AXES, None),
        ),
        out_specs=(
            P("expert", BLOCK_AXES),
            P("expert", BLOCK_AXES),
            P("expert", None),
        ),
        check_vma=False,
    )
```

```python
import math

import jax
import jax.numpy as jnp
from jax import lax
from jax.sharding import PartitionSpec as P

gelu_coef = math.sqrt(2.0 / math.pi)
gelu_cubic = 0.044715


def gelu_parts(hidden):
    inner_arg = gelu_coef * (hidden + gelu_cubic * hidden * hidden * hidden)
    tanh_value = jnp.tanh(inner_arg)
    activation = 0.5 * hidden * (1.0 + tanh_value)
    derivative = 0.5 * (1.0 + tanh_value) + 0.5 * hidden * (
        1.0 - tanh_value * tanh_value
    ) * gelu_coef * (1.0 + 3.0 * gelu_cubic * hidden * hidden)
    return (activation, derivative)


def slot_positions(expert_ids, capacity, experts):
    flat_ids = expert_ids.reshape(-1)
    one_hot = (flat_ids[:, None] == jnp.arange(experts, dtype=jnp.int32)[None, :]).astype(jnp.int32)
    earlier = jnp.sum((jnp.cumsum(one_hot, axis=0) - one_hot) * one_hot, axis=1)
    return flat_ids * capacity + earlier


def transposed_product(left, right):
    return lax.dot_general(
        left, right, (((1,), (1,)), ((), ())), preferred_element_type=jnp.float32
    )


BLOCK_AXES = ("sec", "section")


def per_device(tokens, cotangent, expert_ids, gate_values, expand_weight, contract_weight):
    tok_rows, width_share = tokens.shape
    experts = lax.axis_size("expert")
    capacity = 3 * tok_rows // experts
    slot_count = experts * capacity
    expand_local = expand_weight[0]
    contract_local = contract_weight[0]
    full_width = contract_local.shape[1]
    positions = slot_positions(expert_ids, capacity, experts)
    placement_matrix = (
        positions[:, None] == jnp.arange(slot_count, dtype=jnp.int32)[None, :]
    ).astype(jnp.bfloat16)

    lane = 128
    groups = full_width // lane
    chunk_rows = capacity * groups
    pair_to_slot = placement_matrix
    token_to_slot = jnp.sum(
        placement_matrix.reshape(tok_rows, 2, slot_count), axis=1, dtype=jnp.float32
    ).astype(jnp.bfloat16)

    def gather_rows(selector, rows):
        return lax.dot_general(
            selector, rows, (((0,), (0,)), ((), ())), preferred_element_type=jnp.float32
        ).astype(jnp.bfloat16)

    stacked = jnp.stack([tokens, cotangent], axis=1)
    whole_stacked = lax.all_gather(stacked, BLOCK_AXES, axis=2, tiled=True)
    whole_tokens = whole_stacked[:, 0, :].reshape(tok_rows, groups, lane)
    whole_cot = whole_stacked[:, 1, :].reshape(tok_rows, groups, lane)
    whole_grad = (
        gate_values[:, :, None, None] * whole_cot[:, None, :, :].astype(jnp.float32)
    ).astype(jnp.bfloat16)
    send_x = gather_rows(token_to_slot, whole_tokens)
    send_g = gather_rows(pair_to_slot, whole_grad.reshape(2 * tok_rows, groups, lane))
    send_xg = jnp.concatenate(
        [send_x.reshape(experts, chunk_rows, lane), send_g.reshape(experts, chunk_rows, lane)],
        axis=1,
    )
    recv_xg = lax.all_to_all(send_xg, "expert", split_axis=0, concat_axis=0, tiled=True)
    recv_x = recv_xg[:, :chunk_rows].reshape(slot_count, groups, lane)
    recv_g = recv_xg[:, chunk_rows:].reshape(slot_count, groups, lane)
    expand_3d = expand_local.reshape(groups, lane, -1)
    contract_3d = contract_local.reshape(-1, groups, lane)
    hidden = lax.dot_general(
        recv_x, expand_3d, (((1, 2), (0, 1)), ((), ())), preferred_element_type=jnp.float32
    )
    activation, derivative = gelu_parts(hidden)
    activation = activation.astype(jnp.bfloat16)
    out_part = lax.dot_general(
        activation, contract_3d, (((1,), (0,)), ((), ())), preferred_element_type=jnp.float32
    ).astype(jnp.bfloat16)
    grad_activation = lax.dot_general(
        recv_g, contract_3d, (((1, 2), (1, 2)), ((), ())), preferred_element_type=jnp.float32
    )
    grad_hidden = (grad_activation * derivative).astype(jnp.bfloat16)
    back_part = lax.dot_general(
        grad_hidden, expand_3d, (((1,), (2,)), ((), ())), preferred_element_type=jnp.float32
    ).astype(jnp.bfloat16)
    send_parts = jnp.concatenate(
        [out_part.reshape(experts, chunk_rows, lane), back_part.reshape(experts, chunk_rows, lane)],
        axis=1,
    )
    recv_parts = lax.all_to_all(send_parts, "expert", split_axis=0, concat_axis=0, tiled=True)
    returned_out = recv_parts[:, :chunk_rows].reshape(slot_count, groups, lane)
    returned_back = recv_parts[:, chunk_rows:].reshape(slot_count, groups, lane)
    out_pairs = lax.dot_general(
        pair_to_slot, returned_out, (((1,), (0,)), ((), ())), preferred_element_type=jnp.float32
    ).reshape(tok_rows, 2, groups, lane)
    back_pairs = lax.dot_general(
        pair_to_slot, returned_back, (((1,), (0,)), ((), ())), preferred_element_type=jnp.float32
    ).reshape(tok_rows, 2, groups, lane)
    combined_part = jnp.sum(gate_values[:, :, None, None] * out_pairs, axis=1)
    input_part = back_pairs[:, 0] + back_pairs[:, 1]
    partial_dots = jnp.sum(
        whole_cot[:, None, :, :].astype(jnp.float32) * out_pairs, axis=(2, 3)
    )
    reduced = lax.psum_scatter(
        jnp.stack([combined_part, input_part]).astype(jnp.bfloat16).reshape(2, tok_rows, -1),
        BLOCK_AXES,
        scatter_dimension=2,
        tiled=True,
    )
    gate_grad = lax.psum(partial_dots, BLOCK_AXES)
    combined = reduced[0]
    input_grad = reduced[1]
    return (combined, input_grad, gate_grad)


def solution(mesh):
    return jax.shard_map(
        per_device,
        mesh=mesh,
        in_specs=(
            P("expert", BLOCK_AXES),
            P("expert", BLOCK_AXES),
            P("expert", None),
            P("expert", None),
            P("expert", None, BLOCK_AXES),
            P("expert", BLOCK_AXES, None),
        ),
        out_specs=(
            P("expert", BLOCK_AXES),
            P("expert", BLOCK_AXES),
            P("expert", None),
        ),
        check_vma=False,
    )
```

```python
import math

import jax
import jax.numpy as jnp
from jax import lax
from jax.sharding import PartitionSpec as P

gelu_coef = math.sqrt(2.0 / math.pi)
gelu_cubic = 0.044715


def gelu_parts(hidden):
    inner_arg = gelu_coef * (hidden + gelu_cubic * hidden * hidden * hidden)
    tanh_value = jnp.tanh(inner_arg)
    activation = 0.5 * hidden * (1.0 + tanh_value)
    derivative = 0.5 * (1.0 + tanh_value) + 0.5 * hidden * (
        1.0 - tanh_value * tanh_value
    ) * gelu_coef * (1.0 + 3.0 * gelu_cubic * hidden * hidden)
    return (activation, derivative)


def slot_positions(expert_ids, capacity, experts):
    flat_ids = expert_ids.reshape(-1)
    one_hot = (flat_ids[:, None] == jnp.arange(experts, dtype=jnp.int32)[None, :]).astype(jnp.int32)
    earlier = jnp.sum((jnp.cumsum(one_hot, axis=0) - one_hot) * one_hot, axis=1)
    return flat_ids * capacity + earlier


def transposed_product(left, right):
    return lax.dot_general(
        left, right, (((1,), (1,)), ((), ())), preferred_element_type=jnp.float32
    )


BLOCK_AXES = ("sec", "section")


def per_device(tokens, cotangent, expert_ids, gate_values, expand_weight, contract_weight):
    tok_rows, width_share = tokens.shape
    experts = lax.axis_size("expert")
    capacity = 3 * tok_rows // experts
    slot_count = experts * capacity
    expand_local = expand_weight[0]
    contract_local = contract_weight[0]
    full_width = contract_local.shape[1]
    positions = slot_positions(expert_ids, capacity, experts)
    placement_matrix = (
        positions[:, None] == jnp.arange(slot_count, dtype=jnp.int32)[None, :]
    ).astype(jnp.bfloat16)

    lane = 128
    groups = full_width // lane
    chunk_rows = capacity * groups
    pair_to_slot = placement_matrix
    token_to_slot = jnp.sum(
        placement_matrix.reshape(tok_rows, 2, slot_count), axis=1, dtype=jnp.float32
    ).astype(jnp.bfloat16)

    def gather_rows(selector, rows):
        return lax.dot_general(
            selector, rows, (((0,), (0,)), ((), ())), preferred_element_type=jnp.float32
        ).astype(jnp.bfloat16)

    stacked = jnp.stack([tokens, cotangent], axis=1)
    whole_stacked = lax.all_gather(stacked, BLOCK_AXES, axis=2, tiled=True)
    whole_tokens = whole_stacked[:, 0, :].reshape(tok_rows, groups, lane)
    whole_cot = whole_stacked[:, 1, :].reshape(tok_rows, groups, lane)
    whole_grad = (
        gate_values[:, :, None, None] * whole_cot[:, None, :, :].astype(jnp.float32)
    ).astype(jnp.bfloat16)
    send_x = gather_rows(token_to_slot, whole_tokens)
    send_g = gather_rows(pair_to_slot, whole_grad.reshape(2 * tok_rows, groups, lane))
    send_xg = jnp.concatenate(
        [send_x.reshape(experts, chunk_rows, lane), send_g.reshape(experts, chunk_rows, lane)],
        axis=1,
    )
    recv_xg = lax.all_to_all(send_xg, "expert", split_axis=0, concat_axis=0, tiled=True)
    recv_x = recv_xg[:, :chunk_rows].reshape(slot_count, groups, lane)
    recv_g = recv_xg[:, chunk_rows:].reshape(slot_count, groups, lane)
    expand_3d = expand_local.reshape(groups, lane, -1)
    contract_3d = contract_local.reshape(-1, groups, lane)
    hidden = lax.dot_general(
        recv_x, expand_3d, (((1, 2), (0, 1)), ((), ())), preferred_element_type=jnp.float32
    )
    activation, derivative = gelu_parts(hidden)
    activation = activation.astype(jnp.bfloat16)
    out_part = lax.dot_general(
        activation, contract_3d, (((1,), (0,)), ((), ())), preferred_element_type=jnp.float32
    ).astype(jnp.bfloat16)
    grad_activation = lax.dot_general(
        recv_g, contract_3d, (((1, 2), (1, 2)), ((), ())), preferred_element_type=jnp.float32
    )
    grad_hidden = (grad_activation * derivative).astype(jnp.bfloat16)
    back_part = lax.dot_general(
        grad_hidden, expand_3d, (((1,), (2,)), ((), ())), preferred_element_type=jnp.float32
    ).astype(jnp.bfloat16)
    send_parts = jnp.concatenate(
        [out_part.reshape(experts, chunk_rows, lane), back_part.reshape(experts, chunk_rows, lane)],
        axis=1,
    )
    recv_parts = lax.all_to_all(send_parts, "expert", split_axis=0, concat_axis=0, tiled=True)
    returned_out = recv_parts[:, :chunk_rows].reshape(slot_count, groups, lane)
    returned_back = recv_parts[:, chunk_rows:].reshape(slot_count, groups, lane)
    pair_gates = jnp.sum(
        placement_matrix.reshape(tok_rows, 2, slot_count).astype(jnp.float32)
        * gate_values[:, :, None],
        axis=1,
    )
    gate_hi = pair_gates.astype(jnp.bfloat16)
    gate_lo = (pair_gates - gate_hi.astype(jnp.float32)).astype(jnp.bfloat16)

    def pick_rows(selector, rows):
        return lax.dot_general(
            selector, rows, (((1,), (0,)), ((), ())), preferred_element_type=jnp.float32
        )

    combined_part = pick_rows(gate_hi, returned_out) + pick_rows(gate_lo, returned_out)
    input_part = pick_rows(token_to_slot, returned_back)
    slot_dots = lax.dot_general(
        whole_cot, returned_out, (((1, 2), (1, 2)), ((), ())), preferred_element_type=jnp.float32
    )
    partial_dots = jnp.sum(
        placement_matrix.reshape(tok_rows, 2, slot_count).astype(jnp.float32)
        * slot_dots[:, None, :],
        axis=2,
    )
    reduced = lax.psum_scatter(
        jnp.stack([combined_part, input_part]).astype(jnp.bfloat16).reshape(2, tok_rows, -1),
        BLOCK_AXES,
        scatter_dimension=2,
        tiled=True,
    )
    gate_grad = lax.psum(partial_dots, BLOCK_AXES)
    combined = reduced[0]
    input_grad = reduced[1]
    return (combined, input_grad, gate_grad)


def solution(mesh):
    return jax.shard_map(
        per_device,
        mesh=mesh,
        in_specs=(
            P("expert", BLOCK_AXES),
            P("expert", BLOCK_AXES),
            P("expert", None),
            P("expert", None),
            P("expert", None, BLOCK_AXES),
            P("expert", BLOCK_AXES, None),
        ),
        out_specs=(
            P("expert", BLOCK_AXES),
            P("expert", BLOCK_AXES),
            P("expert", None),
        ),
        check_vma=False,
    )
```

```python
import math

import jax
import jax.numpy as jnp
from jax import lax
from jax.sharding import PartitionSpec as P

gelu_coef = math.sqrt(2.0 / math.pi)
gelu_cubic = 0.044715


def gelu_parts(hidden):
    inner_arg = gelu_coef * (hidden + gelu_cubic * hidden * hidden * hidden)
    tanh_value = jnp.tanh(inner_arg)
    activation = 0.5 * hidden * (1.0 + tanh_value)
    derivative = 0.5 * (1.0 + tanh_value) + 0.5 * hidden * (
        1.0 - tanh_value * tanh_value
    ) * gelu_coef * (1.0 + 3.0 * gelu_cubic * hidden * hidden)
    return (activation, derivative)


def slot_positions(expert_ids, capacity, experts):
    flat_ids = expert_ids.reshape(-1)
    one_hot = (flat_ids[:, None] == jnp.arange(experts, dtype=jnp.int32)[None, :]).astype(jnp.int32)
    earlier = jnp.sum((jnp.cumsum(one_hot, axis=0) - one_hot) * one_hot, axis=1)
    return flat_ids * capacity + earlier


def transposed_product(left, right):
    return lax.dot_general(
        left, right, (((1,), (1,)), ((), ())), preferred_element_type=jnp.float32
    )


BLOCK_AXES = ("sec", "section")


def per_device(tokens, cotangent, expert_ids, gate_values, expand_weight, contract_weight):
    tok_rows, width_share = tokens.shape
    experts = lax.axis_size("expert")
    capacity = 3 * tok_rows // experts
    slot_count = experts * capacity
    expand_local = expand_weight[0]
    contract_local = contract_weight[0]
    full_width = contract_local.shape[1]
    positions = slot_positions(expert_ids, capacity, experts)
    placement_matrix = (
        positions[:, None] == jnp.arange(slot_count, dtype=jnp.int32)[None, :]
    ).astype(jnp.bfloat16)

    lane = 128
    groups = full_width // lane
    chunk_rows = capacity * groups
    pair_to_slot = placement_matrix
    token_to_slot = jnp.sum(
        placement_matrix.reshape(tok_rows, 2, slot_count), axis=1, dtype=jnp.float32
    ).astype(jnp.bfloat16)

    def gather_rows(selector, rows):
        return lax.dot_general(
            selector, rows, (((0,), (0,)), ((), ())), preferred_element_type=jnp.float32
        ).astype(jnp.bfloat16)

    stacked = jnp.stack([tokens, cotangent], axis=1)
    whole_stacked = lax.all_gather(stacked, BLOCK_AXES, axis=2, tiled=True)
    whole_tokens = whole_stacked[:, 0, :].reshape(tok_rows, groups, lane)
    whole_cot = whole_stacked[:, 1, :].reshape(tok_rows, groups, lane)
    whole_grad = (
        gate_values[:, :, None, None] * whole_cot[:, None, :, :].astype(jnp.float32)
    ).astype(jnp.bfloat16)
    send_x = gather_rows(token_to_slot, whole_tokens)
    send_g = gather_rows(pair_to_slot, whole_grad.reshape(2 * tok_rows, groups, lane))
    send_xg = jnp.concatenate(
        [send_x.reshape(experts, chunk_rows, lane), send_g.reshape(experts, chunk_rows, lane)],
        axis=1,
    )
    recv_xg = lax.all_to_all(send_xg, "expert", split_axis=0, concat_axis=0, tiled=True)
    recv_x = recv_xg[:, :chunk_rows].reshape(slot_count, groups, lane)
    recv_g = recv_xg[:, chunk_rows:].reshape(slot_count, groups, lane)
    expand_3d = expand_local.reshape(groups, lane, -1)
    contract_3d = contract_local.reshape(-1, groups, lane)
    hidden = lax.dot_general(
        recv_x, expand_3d, (((1, 2), (0, 1)), ((), ())), preferred_element_type=jnp.float32
    )
    activation, derivative = gelu_parts(hidden)
    activation = activation.astype(jnp.bfloat16)
    out_part = lax.dot_general(
        activation, contract_3d, (((1,), (0,)), ((), ())), preferred_element_type=jnp.float32
    ).astype(jnp.bfloat16)
    grad_activation = lax.dot_general(
        recv_g, contract_3d, (((1, 2), (1, 2)), ((), ())), preferred_element_type=jnp.float32
    )
    grad_hidden = (grad_activation * derivative).astype(jnp.bfloat16)
    back_part = lax.dot_general(
        grad_hidden, expand_3d, (((1,), (2,)), ((), ())), preferred_element_type=jnp.float32
    ).astype(jnp.bfloat16)
    send_parts = jnp.concatenate(
        [out_part.reshape(experts, chunk_rows, lane), back_part.reshape(experts, chunk_rows, lane)],
        axis=1,
    )
    recv_parts = lax.all_to_all(send_parts, "expert", split_axis=0, concat_axis=0, tiled=True)
    returned_out = recv_parts[:, :chunk_rows].reshape(slot_count, groups, lane)
    returned_back = recv_parts[:, chunk_rows:].reshape(slot_count, groups, lane)
    pair_gates = jnp.sum(
        placement_matrix.reshape(tok_rows, 2, slot_count).astype(jnp.float32)
        * gate_values[:, :, None],
        axis=1,
    )
    gate_hi = pair_gates.astype(jnp.bfloat16)
    gate_lo = (pair_gates - gate_hi.astype(jnp.float32)).astype(jnp.bfloat16)

    def pick_rows(selector, rows):
        return lax.dot_general(
            selector, rows, (((1,), (0,)), ((), ())), preferred_element_type=jnp.float32
        )

    combined_part = pick_rows(gate_hi, returned_out) + pick_rows(gate_lo, returned_out)
    input_part = pick_rows(token_to_slot, returned_back)
    slot_dots = lax.dot_general(
        whole_cot, returned_out, (((1, 2), (1, 2)), ((), ())), preferred_element_type=jnp.float32
    )
    partial_dots = jnp.sum(
        placement_matrix.reshape(tok_rows, 2, slot_count).astype(jnp.float32)
        * slot_dots[:, None, :],
        axis=2,
    )
    block_count = full_width // width_share
    to_reduce = jnp.stack([combined_part, input_part]).astype(jnp.bfloat16)
    reduced_blocks = lax.all_to_all(
        to_reduce.reshape(2, tok_rows, block_count, width_share), BLOCK_AXES, 2, 2, tiled=True
    )
    reduced = jnp.sum(reduced_blocks.astype(jnp.float32), axis=2).astype(jnp.bfloat16)
    gate_grad = lax.psum(partial_dots, BLOCK_AXES)
    combined = reduced[0]
    input_grad = reduced[1]
    return (combined, input_grad, gate_grad)


def solution(mesh):
    return jax.shard_map(
        per_device,
        mesh=mesh,
        in_specs=(
            P("expert", BLOCK_AXES),
            P("expert", BLOCK_AXES),
            P("expert", None),
            P("expert", None),
            P("expert", None, BLOCK_AXES),
            P("expert", BLOCK_AXES, None),
        ),
        out_specs=(
            P("expert", BLOCK_AXES),
            P("expert", BLOCK_AXES),
            P("expert", None),
        ),
        check_vma=False,
    )
```

```python
import math

import jax
import jax.numpy as jnp
from jax import lax
from jax.sharding import PartitionSpec as P

gelu_coef = math.sqrt(2.0 / math.pi)
gelu_cubic = 0.044715


def gelu_parts(hidden):
    inner_arg = gelu_coef * (hidden + gelu_cubic * hidden * hidden * hidden)
    tanh_value = jnp.tanh(inner_arg)
    activation = 0.5 * hidden * (1.0 + tanh_value)
    derivative = 0.5 * (1.0 + tanh_value) + 0.5 * hidden * (
        1.0 - tanh_value * tanh_value
    ) * gelu_coef * (1.0 + 3.0 * gelu_cubic * hidden * hidden)
    return (activation, derivative)


def slot_positions(expert_ids, capacity, experts):
    flat_ids = expert_ids.reshape(-1)
    one_hot = (flat_ids[:, None] == jnp.arange(experts, dtype=jnp.int32)[None, :]).astype(jnp.int32)
    earlier = jnp.sum((jnp.cumsum(one_hot, axis=0) - one_hot) * one_hot, axis=1)
    return flat_ids * capacity + earlier


def transposed_product(left, right):
    return lax.dot_general(
        left, right, (((1,), (1,)), ((), ())), preferred_element_type=jnp.float32
    )


BLOCK_AXES = ("sec", "section")


def per_device(tokens, cotangent, expert_ids, gate_values, expand_weight, contract_weight):
    tok_rows, width_share = tokens.shape
    experts = lax.axis_size("expert")
    capacity = 3 * tok_rows // experts
    slot_count = experts * capacity
    expand_local = expand_weight[0]
    contract_local = contract_weight[0]
    full_width = contract_local.shape[1]
    positions = slot_positions(expert_ids, capacity, experts)
    placement_matrix = (
        positions[:, None] == jnp.arange(slot_count, dtype=jnp.int32)[None, :]
    ).astype(jnp.bfloat16)

    lane = 128
    groups = full_width // lane
    chunk_rows = capacity * groups
    pair_to_slot = placement_matrix
    token_to_slot = jnp.sum(
        placement_matrix.reshape(tok_rows, 2, slot_count), axis=1, dtype=jnp.float32
    ).astype(jnp.bfloat16)

    def gather_rows(selector, rows):
        return lax.dot_general(
            selector, rows, (((0,), (0,)), ((), ())), preferred_element_type=jnp.float32
        ).astype(jnp.bfloat16)

    stacked = jnp.stack([tokens, cotangent], axis=1)
    whole_stacked = lax.all_gather(stacked, BLOCK_AXES, axis=2, tiled=True)
    whole_tokens = whole_stacked[:, 0, :].reshape(tok_rows, groups, lane)
    whole_cot = whole_stacked[:, 1, :].reshape(tok_rows, groups, lane)
    gate_slot = jnp.sum(
        jnp.where(pair_to_slot > 0, gate_values.reshape(-1)[:, None], 0.0), axis=0
    )
    send_x = gather_rows(token_to_slot, whole_tokens)
    cot_slot = gather_rows(token_to_slot, whole_cot)
    send_g = (gate_slot[:, None, None] * cot_slot.astype(jnp.float32)).astype(jnp.bfloat16)
    send_xg = jnp.concatenate(
        [send_x.reshape(experts, chunk_rows, lane), send_g.reshape(experts, chunk_rows, lane)],
        axis=1,
    )
    recv_xg = lax.all_to_all(send_xg, "expert", split_axis=0, concat_axis=0, tiled=True)
    recv_x = recv_xg[:, :chunk_rows].reshape(slot_count, groups, lane)
    recv_g = recv_xg[:, chunk_rows:].reshape(slot_count, groups, lane)
    expand_3d = expand_local.reshape(groups, lane, -1)
    contract_3d = contract_local.reshape(-1, groups, lane)
    hidden = lax.dot_general(
        recv_x, expand_3d, (((1, 2), (0, 1)), ((), ())), preferred_element_type=jnp.float32
    )
    activation, derivative = gelu_parts(hidden)
    activation = activation.astype(jnp.bfloat16)
    out_part = lax.dot_general(
        activation, contract_3d, (((1,), (0,)), ((), ())), preferred_element_type=jnp.float32
    ).astype(jnp.bfloat16)
    grad_activation = lax.dot_general(
        recv_g, contract_3d, (((1, 2), (1, 2)), ((), ())), preferred_element_type=jnp.float32
    )
    grad_hidden = (grad_activation * derivative).astype(jnp.bfloat16)
    back_part = lax.dot_general(
        grad_hidden, expand_3d, (((1,), (2,)), ((), ())), preferred_element_type=jnp.float32
    ).astype(jnp.bfloat16)
    send_parts = jnp.concatenate(
        [out_part.reshape(experts, chunk_rows, lane), back_part.reshape(experts, chunk_rows, lane)],
        axis=1,
    )
    recv_parts = lax.all_to_all(send_parts, "expert", split_axis=0, concat_axis=0, tiled=True)
    returned_out = recv_parts[:, :chunk_rows].reshape(slot_count, groups, lane)
    returned_back = recv_parts[:, chunk_rows:].reshape(slot_count, groups, lane)
    pair_gates = jnp.sum(
        placement_matrix.reshape(tok_rows, 2, slot_count).astype(jnp.float32)
        * gate_values[:, :, None],
        axis=1,
    )
    gate_hi = pair_gates.astype(jnp.bfloat16)
    gate_lo = (pair_gates - gate_hi.astype(jnp.float32)).astype(jnp.bfloat16)

    def pick_rows(selector, rows):
        return lax.dot_general(
            selector, rows, (((1,), (0,)), ((), ())), preferred_element_type=jnp.float32
        )

    combined_part = pick_rows(gate_hi, returned_out) + pick_rows(gate_lo, returned_out)
    input_part = pick_rows(token_to_slot, returned_back)
    slot_dots = lax.dot_general(
        whole_cot, returned_out, (((1, 2), (1, 2)), ((), ())), preferred_element_type=jnp.float32
    )
    partial_dots = jnp.sum(
        placement_matrix.reshape(tok_rows, 2, slot_count).astype(jnp.float32)
        * slot_dots[:, None, :],
        axis=2,
    )
    reduced = lax.psum_scatter(
        jnp.stack([combined_part, input_part]).astype(jnp.bfloat16).reshape(2, tok_rows, -1),
        BLOCK_AXES,
        scatter_dimension=2,
        tiled=True,
    )
    gate_grad = lax.psum(partial_dots, BLOCK_AXES)
    combined = reduced[0]
    input_grad = reduced[1]
    return (combined, input_grad, gate_grad)


def solution(mesh):
    return jax.shard_map(
        per_device,
        mesh=mesh,
        in_specs=(
            P("expert", BLOCK_AXES),
            P("expert", BLOCK_AXES),
            P("expert", None),
            P("expert", None),
            P("expert", None, BLOCK_AXES),
            P("expert", BLOCK_AXES, None),
        ),
        out_specs=(
            P("expert", BLOCK_AXES),
            P("expert", BLOCK_AXES),
            P("expert", None),
        ),
        check_vma=False,
    )
```

```python
import math

import jax
import jax.numpy as jnp
from jax import lax
from jax.sharding import PartitionSpec as P

gelu_coef = math.sqrt(2.0 / math.pi)
gelu_cubic = 0.044715


def gelu_parts(hidden):
    inner_arg = gelu_coef * (hidden + gelu_cubic * hidden * hidden * hidden)
    tanh_value = jnp.tanh(inner_arg)
    activation = 0.5 * hidden * (1.0 + tanh_value)
    derivative = 0.5 * (1.0 + tanh_value) + 0.5 * hidden * (
        1.0 - tanh_value * tanh_value
    ) * gelu_coef * (1.0 + 3.0 * gelu_cubic * hidden * hidden)
    return (activation, derivative)


def slot_positions(expert_ids, capacity, experts):
    flat_ids = expert_ids.reshape(-1)
    one_hot = (flat_ids[:, None] == jnp.arange(experts, dtype=jnp.int32)[None, :]).astype(jnp.int32)
    earlier = jnp.sum((jnp.cumsum(one_hot, axis=0) - one_hot) * one_hot, axis=1)
    return flat_ids * capacity + earlier


def transposed_product(left, right):
    return lax.dot_general(
        left, right, (((1,), (1,)), ((), ())), preferred_element_type=jnp.float32
    )


BLOCK_AXES = ("sec", "section")


def per_device(tokens, cotangent, expert_ids, gate_values, expand_weight, contract_weight):
    tok_rows, width_share = tokens.shape
    experts = lax.axis_size("expert")
    capacity = 3 * tok_rows // experts
    slot_count = experts * capacity
    expand_local = expand_weight[0]
    contract_local = contract_weight[0]
    full_width = contract_local.shape[1]
    positions = slot_positions(expert_ids, capacity, experts)
    placement_matrix = (
        positions[:, None] == jnp.arange(slot_count, dtype=jnp.int32)[None, :]
    ).astype(jnp.bfloat16)

    lane = 128
    groups = full_width // lane
    chunk_rows = capacity * groups
    pair_to_slot = placement_matrix
    token_to_slot = jnp.sum(
        placement_matrix.reshape(tok_rows, 2, slot_count), axis=1, dtype=jnp.float32
    ).astype(jnp.bfloat16)

    def gather_rows(selector, rows):
        return lax.dot_general(
            selector, rows, (((0,), (0,)), ((), ())), preferred_element_type=jnp.float32
        ).astype(jnp.bfloat16)

    stacked = jnp.stack([tokens, cotangent], axis=1)
    whole_stacked = lax.all_gather(stacked, BLOCK_AXES, axis=2, tiled=True)
    whole_cot = whole_stacked[:, 1, :].reshape(tok_rows, groups, lane)
    gate_slot = jnp.sum(
        jnp.where(pair_to_slot > 0, gate_values.reshape(-1)[:, None], 0.0), axis=0
    )
    stream_scale = jnp.stack([jnp.ones_like(gate_slot), gate_slot], axis=1)
    slot_rows = lax.dot_general(
        token_to_slot,
        whole_stacked.reshape(tok_rows, 2, groups, lane),
        (((0,), (0,)), ((), ())),
        preferred_element_type=jnp.float32,
    )
    send_xg = (stream_scale[:, :, None, None] * slot_rows).astype(jnp.bfloat16)
    recv_xg = lax.all_to_all(
        send_xg.reshape(experts, 2 * chunk_rows, lane), "expert", split_axis=0, concat_axis=0,
        tiled=True,
    ).reshape(slot_count, 2, groups, lane)
    recv_x = recv_xg[:, 0]
    recv_g = recv_xg[:, 1]
    expand_3d = expand_local.reshape(groups, lane, -1)
    contract_3d = contract_local.reshape(-1, groups, lane)
    hidden = lax.dot_general(
        recv_x, expand_3d, (((1, 2), (0, 1)), ((), ())), preferred_element_type=jnp.float32
    )
    activation, derivative = gelu_parts(hidden)
    activation = activation.astype(jnp.bfloat16)
    out_part = lax.dot_general(
        activation, contract_3d, (((1,), (0,)), ((), ())), preferred_element_type=jnp.float32
    ).astype(jnp.bfloat16)
    grad_activation = lax.dot_general(
        recv_g, contract_3d, (((1, 2), (1, 2)), ((), ())), preferred_element_type=jnp.float32
    )
    grad_hidden = (grad_activation * derivative).astype(jnp.bfloat16)
    back_part = lax.dot_general(
        grad_hidden, expand_3d, (((1,), (2,)), ((), ())), preferred_element_type=jnp.float32
    ).astype(jnp.bfloat16)
    send_parts = jnp.concatenate(
        [out_part.reshape(experts, chunk_rows, lane), back_part.reshape(experts, chunk_rows, lane)],
        axis=1,
    )
    recv_parts = lax.all_to_all(send_parts, "expert", split_axis=0, concat_axis=0, tiled=True)
    returned_out = recv_parts[:, :chunk_rows].reshape(slot_count, groups, lane)
    returned_back = recv_parts[:, chunk_rows:].reshape(slot_count, groups, lane)
    pair_gates = jnp.sum(
        placement_matrix.reshape(tok_rows, 2, slot_count).astype(jnp.float32)
        * gate_values[:, :, None],
        axis=1,
    )
    gate_hi = pair_gates.astype(jnp.bfloat16)
    gate_lo = (pair_gates - gate_hi.astype(jnp.float32)).astype(jnp.bfloat16)

    def pick_rows(selector, rows):
        return lax.dot_general(
            selector, rows, (((1,), (0,)), ((), ())), preferred_element_type=jnp.float32
        )

    combined_part = pick_rows(gate_hi, returned_out) + pick_rows(gate_lo, returned_out)
    input_part = pick_rows(token_to_slot, returned_back)
    slot_dots = lax.dot_general(
        whole_cot, returned_out, (((1, 2), (1, 2)), ((), ())), preferred_element_type=jnp.float32
    )
    partial_dots = jnp.sum(
        placement_matrix.reshape(tok_rows, 2, slot_count).astype(jnp.float32)
        * slot_dots[:, None, :],
        axis=2,
    )
    reduced = lax.psum_scatter(
        jnp.stack([combined_part, input_part]).astype(jnp.bfloat16).reshape(2, tok_rows, -1),
        BLOCK_AXES,
        scatter_dimension=2,
        tiled=True,
    )
    gate_grad = lax.psum(partial_dots, BLOCK_AXES)
    combined = reduced[0]
    input_grad = reduced[1]
    return (combined, input_grad, gate_grad)


def solution(mesh):
    return jax.shard_map(
        per_device,
        mesh=mesh,
        in_specs=(
            P("expert", BLOCK_AXES),
            P("expert", BLOCK_AXES),
            P("expert", None),
            P("expert", None),
            P("expert", None, BLOCK_AXES),
            P("expert", BLOCK_AXES, None),
        ),
        out_specs=(
            P("expert", BLOCK_AXES),
            P("expert", BLOCK_AXES),
            P("expert", None),
        ),
        check_vma=False,
    )
```
